512 devices in a mesh: context: 32 (over x_hi, y, core), tensor: 16 (over z, x_lo).
Axes of the slice: x: 4 (x_hi: 2, x_lo: 2; x = x_hi * 2 + x_lo), y: 8, z: 8, core: 2. Of those that a mesh axis runs over, the one named last changes fastest.
Arguments:
- projected: bfloat16 [3, 12288, 8192], P(None, 'context', 'tensor'), may hold values from -6 to 6
- taps: float32 [3, 3, 8192], P(None, None, 'tensor'), may hold values from -4 to 4
- filters: bfloat16 [512, 128], P('tensor'), may hold values from -0.5 to 0.5
- skip: float32 [8192], P('tensor'), may hold values from -4 to 4
- out_weight: bfloat16 [8192, 8192], P('tensor', 'context'), may hold values from -0.125 to 0.125
- positions: int32 [128], replicated, may hold values from 0 to 12287
Outputs:
- mixed: bfloat16 [12288, 8192], P('context', 'tensor')
- variant_states: bfloat16 [128, 8192], P('context', 'tensor')
The draws below stay inside these ranges and needn't reach their ends.
All inputs are finite; a program needn't handle non-finite values.
Results may differ from the reference program's by a relative error of at most 0.018.
Values may be sent and summed in bfloat16 or wider, within the bound.
No kernel may reach another device: no remote copies, remote signals or barrier semaphores. Data moves between devices by JAX's collectives and lax.ppermute only.
A program may use at most 128 MiB of HBM per device.

```python
import jax
import jax.numpy as jnp
from jax import lax

D = 8192
FLT = 128
GROUP = 16
SHORT = 3
GROUPS = 512
TOKENS = 12288
VARIANTS = 128
N_TENSOR = 16


def touch_ends(entries, own_key, low, top_value):
    extent = entries.shape
    spot = [jax.random.randint(jax.random.fold_in(own_key, axis), (), 0, extent[axis]) for axis in range(len(extent))]
    entries = entries.at[tuple(spot)].set(low)
    longest = extent.index(max(extent))
    spot[longest] = (spot[longest] + 1) % extent[longest]
    return entries.at[tuple(spot)].set(top_value)


def raised(array, stream_key, source, target, blocks, factor):
    owner, partner = [(jnp.arange(array.shape[axis_at]) // (array.shape[axis_at] // blocks)).reshape([-1 if axis == axis_at else 1 for axis in range(array.ndim)]) for axis_at in (source, target)]
    chosen = jax.random.permutation(stream_key, blocks)[partner]
    strong = (owner == chosen) | (owner == (partner + blocks // 2) % blocks)
    return jnp.where(strong, factor * array, array)


def block_levels(key, shape, cuts, low, top_value):
    def one(axis_at, blocks):
        heights = jax.random.uniform(jax.random.fold_in(jax.random.fold_in(key, 6), axis_at), (blocks,), jnp.float32, low / len(cuts), top_value / len(cuts))
        return jnp.repeat(jnp.exp(heights), shape[axis_at] // blocks).reshape((-1,) + (1,) * (len(shape) - axis_at - 1))

    level = one(*cuts[0])
    for cut in cuts[1:]:
        level = level * one(*cut)
    return level


def gaussian(stream_key, dims, deviation, reach, cuts=(), dtype=jnp.bfloat16):
    entries = deviation * jax.random.normal(stream_key, dims, jnp.float32)
    if cuts:
        entries = entries * block_levels(stream_key, dims, cuts, -0.22, 0.18)
    return jnp.clip(entries, -reach, reach).astype(dtype)


def gaussian_with(key, dims, scale, most, cuts, heavy, held_as=jnp.bfloat16):
    array = scale * jax.random.normal(key, dims, jnp.float32)
    if cuts:
        array = array * block_levels(key, dims, cuts, -0.22, 0.18)
    return jnp.clip(raised(array, jax.random.fold_in(key, 3), *heavy), -most, most).astype(held_as)


def setup_inputs(seed: int = 0) -> dict:
    seeds = jax.random.split(jax.random.key(seed), 7)
    return {
        "projected": gaussian(seeds[0], (3, TOKENS, D), 1.0, 6.0, ((1, 32), (2, 16))),
        "taps": gaussian(seeds[1], (3, SHORT, D), 0.6, 4.0, ((2, 16),), jnp.float32),
        "filters": gaussian(seeds[2], (GROUPS, FLT), FLT ** -0.5, 0.5, ((0, 16),)),
        "skip": gaussian(seeds[3], (D,), 1.0, 4.0, ((0, 16),), jnp.float32),
        "out_weight": gaussian_with(seeds[4], (D, D), D ** -0.5, 0.125, ((0, 16), (1, 32)), (0, 1, 32, 2.75)),
        "positions": touch_ends(jax.random.randint(seeds[5], (VARIANTS,), 0, TOKENS), jax.random.fold_in(seeds[5], 1), 0, TOKENS - 1).astype(jnp.int32),
    }


def reference(projected, taps, filters, skip, out_weight, positions):
    inputs = projected.astype(jnp.float32)
    padded = jnp.pad(inputs, ((0, 0), (SHORT - 1, 0), (0, 0)))
    feat = jnp.zeros_like(inputs)
    for lag in range(SHORT):
        feat = feat + taps[:, lag, None, :] * padded[:, SHORT - 1 - lag:SHORT - 1 - lag + TOKENS, :]
    query = feat[0]
    product = (feat[1] * feat[2]).astype(jnp.bfloat16)
    product_f = product.astype(jnp.float32)
    per_channel = jnp.repeat(filters.astype(jnp.float32), GROUP, axis=0)
    shifted = jnp.pad(product_f, ((FLT - 1, 0), (0, 0)))

    def add_tap(lag, total):
        window = lax.dynamic_slice_in_dim(shifted, FLT - 1 - lag, TOKENS, 0)
        column = lax.dynamic_slice_in_dim(per_channel, lag, 1, 1)[:, 0]
        return total + column[None, :] * window

    conv = lax.fori_loop(0, FLT, add_tap, skip[None, :] * product_f)
    gated = (query * conv).astype(jnp.bfloat16)
    width = D // N_TENSOR
    mixed = jnp.zeros((TOKENS, D), jnp.float32)
    for block in range(N_TENSOR):
        part = jnp.dot(gated[:, block * width:(block + 1) * width], out_weight[block * width:(block + 1) * width, :], preferred_element_type=jnp.float32)
        mixed = mixed + part.astype(jnp.bfloat16).astype(jnp.float32)
    mixed_out = mixed.astype(jnp.bfloat16)
    variant_states = jnp.take(mixed_out, positions, axis=0)
    return mixed_out, variant_states
```

```python
import jax
import jax.numpy as jnp
from jax import lax
from jax.sharding import PartitionSpec as P

FLT = 128
GROUP = 16
SHORT = 3


def shifted(array, axis, by):
    size = lax.axis_size(axis)
    pairs = [(i, i + by) for i in range(size) if 0 <= i + by < size]
    return lax.ppermute(array, axis, pairs)


def halving_scatter(rows, axis):
    size = lax.axis_size(axis)
    if size & (size - 1) or rows.shape[0] % size:
        return lax.psum_scatter(rows, axis, scatter_dimension=0, tiled=True)
    me = lax.axis_index(axis)
    step = size // 2
    while step >= 1:
        half = rows.shape[0] // 2
        bit = (me // step) % 2
        keep = lax.dynamic_slice_in_dim(rows, bit * half, half, 0)
        send = lax.dynamic_slice_in_dim(rows, (1 - bit) * half, half, 0)
        pairs = [(i, i ^ step) for i in range(size)]
        rows = keep + lax.ppermute(send, axis, pairs)
        step //= 2
    return rows


def short_filter(extended, weights, count):
    lags = SHORT - 1
    total = jnp.zeros((extended.shape[0], count, extended.shape[2]), jnp.float32)
    for lag in range(SHORT):
        total = total + weights[:, lag, None, :] * extended[
            :, lags - lag : lags - lag + count, :
        ].astype(jnp.float32)
    return total


def banded_filters(filters, rows):
    local_groups = filters.shape[0]
    span = FLT - 1 + rows
    reversed_taps = jnp.flip(filters, axis=1)
    padded_taps = jnp.concatenate(
        [reversed_taps, jnp.zeros((local_groups, rows), filters.dtype)], axis=1
    )
    tiled = jnp.tile(padded_taps, (1, rows))
    return tiled[:, : rows * span].reshape(local_groups, rows, span)


def on_device(projected, taps, filters, skip, out_weight, positions):
    rows = projected.shape[1]
    width = projected.shape[2]
    lags = SHORT - 1
    reach = FLT - 1
    rim = shifted(projected[:, rows - lags :, :], "context", 1)
    feat = short_filter(jnp.concatenate([rim, projected], axis=1), taps, rows)
    query = feat[0]
    product = (feat[1] * feat[2]).astype(jnp.bfloat16)
    prior = shifted(product[rows - reach :], "context", 1)
    extended = jnp.concatenate([prior, product], axis=0)
    span = reach + rows
    toeplitz = banded_filters(filters, rows)
    local_groups = filters.shape[0]
    conv = jnp.einsum(
        "gim,mgc->igc",
        toeplitz,
        extended.reshape(span, local_groups, GROUP),
        preferred_element_type=jnp.float32,
    ).reshape(rows, width)
    conv = conv + skip[None, :] * product.astype(jnp.float32)
    gated = (query * conv).astype(jnp.bfloat16)
    terms = jnp.dot(
        gated,
        lax.all_gather(out_weight, "context", axis=1, tiled=True),
        preferred_element_type=jnp.float32,
    )
    mixed = lax.psum_scatter(terms.astype(jnp.bfloat16), "tensor", scatter_dimension=1, tiled=True)
    offset = lax.axis_index("context") * rows
    local_sites = positions - offset
    one_hot = (local_sites[:, None] == jnp.arange(rows, dtype=jnp.int32)[None, :]).astype(
        jnp.bfloat16
    )
    picked_terms = jnp.dot(one_hot, mixed, preferred_element_type=jnp.float32)
    variant_states = halving_scatter(picked_terms.astype(jnp.bfloat16), "context")
    return (mixed, variant_states)


def solution(mesh):
    return jax.shard_map(
        on_device,
        mesh=mesh,
        in_specs=(
            P(None, "context", "tensor"),
            P(None, None, "tensor"),
            P("tensor", None),
            P("tensor"),
            P("tensor", "context"),
            P(),
        ),
        out_specs=(P("context", "tensor"), P("context", "tensor")),
        check_vma=False,
    )
```

```python
import jax
import jax.numpy as jnp
from jax import lax
import numpy as np
from jax.sharding import Mesh, PartitionSpec as P

FLT = 128
GROUP = 16
SHORT = 3


def shifted(array, axis, by):
    size = lax.axis_size(axis)
    pairs = [(i, i + by) for i in range(size) if 0 <= i + by < size]
    return lax.ppermute(array, axis, pairs)


def halving_scatter(rows, axis):
    size = lax.axis_size(axis)
    if size & (size - 1) or rows.shape[0] % size:
        return lax.psum_scatter(rows, axis, scatter_dimension=0, tiled=True)
    me = lax.axis_index(axis)
    step = size // 2
    while step >= 1:
        half = rows.shape[0] // 2
        bit = (me // step) % 2
        keep = lax.dynamic_slice_in_dim(rows, bit * half, half, 0)
        send = lax.dynamic_slice_in_dim(rows, (1 - bit) * half, half, 0)
        pairs = [(i, i ^ step) for i in range(size)]
        rows = keep + lax.ppermute(send, axis, pairs)
        step //= 2
    return rows


def short_filter(extended, weights, count):
    lags = SHORT - 1
    total = jnp.zeros((extended.shape[0], count, extended.shape[2]), jnp.float32)
    for lag in range(SHORT):
        total = total + weights[:, lag, None, :] * extended[
            :, lags - lag : lags - lag + count, :
        ].astype(jnp.float32)
    return total


def banded_filters(filters, rows):
    local_groups = filters.shape[0]
    span = FLT - 1 + rows
    reversed_taps = jnp.flip(filters, axis=1)
    padded_taps = jnp.concatenate(
        [reversed_taps, jnp.zeros((local_groups, rows), filters.dtype)], axis=1
    )
    tiled = jnp.tile(padded_taps, (1, rows))
    return tiled[:, : rows * span].reshape(local_groups, rows, span)


def on_device(projected, taps, filters, skip, out_weight, positions):
    rows = projected.shape[1]
    width = projected.shape[2]
    lags = SHORT - 1
    reach = FLT - 1
    rim = shifted(projected[:, rows - lags :, :], "context", 1)
    feat = short_filter(jnp.concatenate([rim, projected], axis=1), taps, rows)
    query = feat[0]
    product = (feat[1] * feat[2]).astype(jnp.bfloat16)
    prior = shifted(product[rows - reach :], "context", 1)
    extended = jnp.concatenate([prior, product], axis=0)
    span = reach + rows
    toeplitz = banded_filters(filters, rows)
    local_groups = filters.shape[0]
    conv = jnp.einsum(
        "gim,mgc->igc",
        toeplitz,
        extended.reshape(span, local_groups, GROUP),
        preferred_element_type=jnp.float32,
    ).reshape(rows, width)
    conv = conv + skip[None, :] * product.astype(jnp.float32)
    gated = (query * conv).astype(jnp.bfloat16)
    terms = jnp.dot(
        gated,
        lax.all_gather(out_weight, "context", axis=1, tiled=True),
        preferred_element_type=jnp.float32,
    )
    mixed = lax.psum_scatter(terms.astype(jnp.bfloat16), "z", scatter_dimension=1, tiled=True)
    mixed = lax.psum_scatter(mixed, "x_lo", scatter_dimension=1, tiled=True)
    offset = lax.axis_index("context") * rows
    local_sites = positions - offset
    one_hot = (local_sites[:, None] == jnp.arange(rows, dtype=jnp.int32)[None, :]).astype(
        jnp.bfloat16
    )
    picked_terms = jnp.dot(one_hot, mixed, preferred_element_type=jnp.float32)
    variant_states = halving_scatter(picked_terms.astype(jnp.bfloat16), "context")
    return (mixed, variant_states)


def split_mesh(mesh):
    devices = np.asarray(mesh.devices)
    context, tensor = devices.shape
    return Mesh(devices.reshape(context, tensor // 2, 2), ("context", "z", "x_lo"))


def solution(mesh):
    tensor = ("z", "x_lo")
    return jax.shard_map(
        on_device,
        mesh=split_mesh(mesh),
        in_specs=(
            P(None, "context", tensor),
            P(None, None, tensor),
            P(tensor, None),
            P(tensor),
            P(tensor, "context"),
            P(),
        ),
        out_specs=(P("context", tensor), P("context", tensor)),
        check_vma=False,
    )
```

```python
import jax
import jax.numpy as jnp
from jax import lax
import numpy as np
from jax.sharding import Mesh, PartitionSpec as P

FLT = 128
GROUP = 16
SHORT = 3


def shifted(array, axis, by):
    size = lax.axis_size(axis)
    pairs = [(i, i + by) for i in range(size) if 0 <= i + by < size]
    return lax.ppermute(array, axis, pairs)


def pair_scatter(block, axis):
    me = lax.axis_index(axis)
    half = block.shape[1] // 2
    keep = lax.dynamic_slice_in_dim(block, me * half, half, 1)
    send = lax.dynamic_slice_in_dim(block, (1 - me) * half, half, 1)
    got = lax.ppermute(send, axis, [(0, 1), (1, 0)])
    return (keep.astype(jnp.float32) + got.astype(jnp.float32)).astype(block.dtype)


def exchange_scatter(rows, axis):
    size = lax.axis_size(axis)
    pieces = rows.reshape(size, rows.shape[0] // size, rows.shape[1])
    pieces = lax.all_to_all(pieces, axis, 0, 0, tiled=True)
    return pieces.astype(jnp.float32).sum(0).astype(rows.dtype)


def short_filter(extended, weights, count):
    lags = SHORT - 1
    total = jnp.zeros((extended.shape[0], count, extended.shape[2]), jnp.float32)
    for lag in range(SHORT):
        total = total + weights[:, lag, None, :] * extended[
            :, lags - lag : lags - lag + count, :
        ].astype(jnp.float32)
    return total


def banded_filters(filters, rows):
    local_groups = filters.shape[0]
    span = FLT - 1 + rows
    reversed_taps = jnp.flip(filters, axis=1)
    padded_taps = jnp.concatenate(
        [reversed_taps, jnp.zeros((local_groups, rows), filters.dtype)], axis=1
    )
    tiled = jnp.tile(padded_taps, (1, rows))
    return tiled[:, : rows * span].reshape(local_groups, rows, span)


def on_device(projected, taps, filters, skip, out_weight, positions):
    rows = projected.shape[1]
    width = projected.shape[2]
    lags = SHORT - 1
    reach = FLT - 1
    rim = shifted(projected[:, rows - lags :, :], "context", 1)
    feat = short_filter(jnp.concatenate([rim, projected], axis=1), taps, rows)
    query = feat[0]
    product = (feat[1] * feat[2]).astype(jnp.bfloat16)
    prior = shifted(product[rows - reach :], "context", 1)
    extended = jnp.concatenate([prior, product], axis=0)
    span = reach + rows
    toeplitz = banded_filters(filters, rows)
    local_groups = filters.shape[0]
    conv = jnp.einsum(
        "gim,mgc->igc",
        toeplitz,
        extended.reshape(span, local_groups, GROUP),
        preferred_element_type=jnp.float32,
    ).reshape(rows, width)
    conv = conv + skip[None, :] * product.astype(jnp.float32)
    gated = (query * conv).astype(jnp.bfloat16)
    terms = jnp.dot(
        gated,
        lax.all_gather(out_weight, "context", axis=1, tiled=True),
        preferred_element_type=jnp.float32,
    )
    mixed = lax.psum_scatter(terms.astype(jnp.bfloat16), "z", scatter_dimension=1, tiled=True)
    mixed = pair_scatter(mixed, "x_lo")
    offset = lax.axis_index("context") * rows
    local_sites = positions - offset
    one_hot = (local_sites[:, None] == jnp.arange(rows, dtype=jnp.int32)[None, :]).astype(
        jnp.bfloat16
    )
    picked_terms = jnp.dot(one_hot, mixed, preferred_element_type=jnp.float32)
    variant_states = exchange_scatter(picked_terms.astype(jnp.bfloat16), "context")
    return (mixed, variant_states)


def split_mesh(mesh):
    devices = np.asarray(mesh.devices)
    context, tensor = devices.shape
    return Mesh(devices.reshape(context, tensor // 2, 2), ("context", "z", "x_lo"))


def solution(mesh):
    tensor = ("z", "x_lo")
    return jax.shard_map(
        on_device,
        mesh=split_mesh(mesh),
        in_specs=(
            P(None, "context", tensor),
            P(None, None, tensor),
            P(tensor, None),
            P(tensor),
            P(tensor, "context"),
            P(),
        ),
        out_specs=(P("context", tensor), P("context", tensor)),
        check_vma=False,
    )
```

```python
import jax
import jax.numpy as jnp
from jax import lax
import numpy as np
from jax.sharding import Mesh, PartitionSpec as P

FLT = 128
GROUP = 16
SHORT = 3


def shifted(array, axis, by):
    size = lax.axis_size(axis)
    pairs = [(i, i + by) for i in range(size) if 0 <= i + by < size]
    return lax.ppermute(array, axis, pairs)


def pair_scatter(block, axis):
    me = lax.axis_index(axis)
    half = block.shape[1] // 2
    keep = lax.dynamic_slice_in_dim(block, me * half, half, 1)
    send = lax.dynamic_slice_in_dim(block, (1 - me) * half, half, 1)
    got = lax.ppermute(send, axis, [(0, 1), (1, 0)])
    return (keep.astype(jnp.float32) + got.astype(jnp.float32)).astype(block.dtype)


def exchange_scatter(rows, axis):
    size = lax.axis_size(axis)
    pieces = rows.reshape(size, rows.shape[0] // size, rows.shape[1])
    pieces = lax.all_to_all(pieces, axis, 0, 0, tiled=True)
    return pieces.astype(jnp.float32).sum(0).astype(rows.dtype)


def short_filter(extended, weights, count):
    lags = SHORT - 1
    total = jnp.zeros((extended.shape[0], count, extended.shape[2]), jnp.float32)
    for lag in range(SHORT):
        total = total + weights[:, lag, None, :] * extended[
            :, lags - lag : lags - lag + count, :
        ].astype(jnp.float32)
    return total


def banded_filters(filters, rows):
    local_groups = filters.shape[0]
    span = FLT - 1 + rows
    reversed_taps = jnp.flip(filters, axis=1)
    padded_taps = jnp.concatenate(
        [reversed_taps, jnp.zeros((local_groups, rows), filters.dtype)], axis=1
    )
    tiled = jnp.tile(padded_taps, (1, rows))
    return tiled[:, : rows * span].reshape(local_groups, rows, span)


def on_device(projected, taps, filters, skip, out_weight, positions):
    rows = projected.shape[1]
    width = projected.shape[2]
    lags = SHORT - 1
    reach = FLT - 1
    rim = shifted(projected[:, rows - lags :, :], "context", 1)
    feat = short_filter(jnp.concatenate([rim, projected], axis=1), taps, rows)
    query = feat[0]
    product = (feat[1] * feat[2]).astype(jnp.bfloat16)
    prior = shifted(product[rows - reach :], "context", 1)
    extended = jnp.concatenate([prior, product], axis=0)
    span = reach + rows
    toeplitz = banded_filters(filters, rows)
    local_groups = filters.shape[0]
    conv = jnp.einsum(
        "gim,mgc->igc",
        toeplitz,
        extended.reshape(span, local_groups, GROUP),
        preferred_element_type=jnp.float32,
    ).reshape(rows, width)
    conv = conv + skip[None, :] * product.astype(jnp.float32)
    gated = (query * conv).astype(jnp.bfloat16)
    terms = jnp.dot(
        gated,
        lax.all_gather(out_weight, "context", axis=1, tiled=True),
        preferred_element_type=jnp.float32,
    )
    partial = lax.psum_scatter(terms.astype(jnp.bfloat16), "z", scatter_dimension=1, tiled=True)
    mixed = pair_scatter(partial, "x_lo")
    offset = lax.axis_index("context") * rows
    local_sites = positions - offset
    one_hot = (local_sites[:, None] == jnp.arange(rows, dtype=jnp.int32)[None, :]).astype(
        jnp.bfloat16
    )
    picked_terms = jnp.dot(one_hot, partial, preferred_element_type=jnp.float32)
    picked = exchange_scatter(picked_terms.astype(jnp.bfloat16), "context")
    variant_states = pair_scatter(picked, "x_lo")
    return (mixed, variant_states)


def split_mesh(mesh):
    devices = np.asarray(mesh.devices)
    context, tensor = devices.shape
    return Mesh(devices.reshape(context, tensor // 2, 2), ("context", "z", "x_lo"))


def solution(mesh):
    tensor = ("z", "x_lo")
    return jax.shard_map(
        on_device,
        mesh=split_mesh(mesh),
        in_specs=(
            P(None, "context", tensor),
            P(None, None, tensor),
            P(tensor, None),
            P(tensor),
            P(tensor, "context"),
            P(),
        ),
        out_specs=(P("context", tensor), P("context", tensor)),
        check_vma=False,
    )
```

```python
import jax
import jax.numpy as jnp
from jax import lax
import numpy as np
from jax.sharding import Mesh, PartitionSpec as P

FLT = 128
GROUP = 16
SHORT = 3


def shifted(array, axis, by):
    size = lax.axis_size(axis)
    pairs = [(i, i + by) for i in range(size) if 0 <= i + by < size]
    return lax.ppermute(array, axis, pairs)


def pair_scatter(block, axis):
    me = lax.axis_index(axis)
    half = block.shape[1] // 2
    keep = lax.dynamic_slice_in_dim(block, me * half, half, 1)
    send = lax.dynamic_slice_in_dim(block, (1 - me) * half, half, 1)
    got = lax.ppermute(send, axis, [(0, 1), (1, 0)])
    return (keep.astype(jnp.float32) + got.astype(jnp.float32)).astype(block.dtype)


def exchange_scatter(rows, axis):
    size = lax.axis_size(axis)
    pieces = rows.reshape(size, rows.shape[0] // size, rows.shape[1])
    pieces = lax.all_to_all(pieces, axis, 0, 0, tiled=True)
    return pieces.astype(jnp.float32).sum(0).astype(rows.dtype)


def short_filter(extended, weights, count):
    lags = SHORT - 1
    total = jnp.zeros((extended.shape[0], count, extended.shape[2]), jnp.float32)
    for lag in range(SHORT):
        total = total + weights[:, lag, None, :] * extended[
            :, lags - lag : lags - lag + count, :
        ].astype(jnp.float32)
    return total


def banded_filters(filters, rows):
    local_groups = filters.shape[0]
    span = FLT - 1 + rows
    reversed_taps = jnp.flip(filters, axis=1)
    padded_taps = jnp.concatenate(
        [reversed_taps, jnp.zeros((local_groups, rows), filters.dtype)], axis=1
    )
    tiled = jnp.tile(padded_taps, (1, rows))
    return tiled[:, : rows * span].reshape(local_groups, rows, span)


def on_device(projected, taps, filters, skip, out_weight, positions):
    rows = projected.shape[1]
    width = projected.shape[2]
    lags = SHORT - 1
    reach = FLT - 1
    rim = shifted(projected[:, rows - lags :, :], "context", 1)
    feat = short_filter(jnp.concatenate([rim, projected], axis=1), taps, rows)
    query = feat[0]
    product = (feat[1] * feat[2]).astype(jnp.bfloat16)
    prior = shifted(product[rows - reach :], "context", 1)
    extended = jnp.concatenate([prior, product], axis=0)
    span = reach + rows
    toeplitz = banded_filters(filters, rows)
    local_groups = filters.shape[0]
    conv = jnp.einsum(
        "gim,mgc->igc",
        toeplitz,
        extended.reshape(span, local_groups, GROUP),
        preferred_element_type=jnp.float32,
    ).reshape(rows, width)
    conv = conv + skip[None, :] * product.astype(jnp.float32)
    gated = lax.optimization_barrier((query * conv).astype(jnp.bfloat16))
    terms = jnp.dot(
        gated,
        lax.all_gather(out_weight, "context", axis=1, tiled=True),
        preferred_element_type=jnp.float32,
    )
    partial = lax.psum_scatter(terms.astype(jnp.bfloat16), "z", scatter_dimension=1, tiled=True)
    mixed = pair_scatter(partial, "x_lo")
    offset = lax.axis_index("context") * rows
    local_sites = positions - offset
    one_hot = (local_sites[:, None] == jnp.arange(rows, dtype=jnp.int32)[None, :]).astype(
        jnp.bfloat16
    )
    picked_terms = jnp.dot(one_hot, partial, preferred_element_type=jnp.float32)
    picked = exchange_scatter(picked_terms.astype(jnp.bfloat16), "context")
    variant_states = pair_scatter(picked, "x_lo")
    return (mixed, variant_states)


def split_mesh(mesh):
    devices = np.asarray(mesh.devices)
    context, tensor = devices.shape
    return Mesh(devices.reshape(context, tensor // 2, 2), ("context", "z", "x_lo"))


def solution(mesh):
    tensor = ("z", "x_lo")
    return jax.shard_map(
        on_device,
        mesh=split_mesh(mesh),
        in_specs=(
            P(None, "context", tensor),
            P(None, None, tensor),
            P(tensor, None),
            P(tensor),
            P(tensor, "context"),
            P(),
        ),
        out_specs=(P("context", tensor), P("context", tensor)),
        check_vma=False,
    )
```

```python
import jax
import jax.numpy as jnp
from jax import lax
import numpy as np
from jax.sharding import Mesh, PartitionSpec as P

FLT = 128
GROUP = 16
SHORT = 3


def shifted(array, axis, by):
    size = lax.axis_size(axis)
    pairs = [(i, i + by) for i in range(size) if 0 <= i + by < size]
    return lax.ppermute(array, axis, pairs)


def pair_scatter(block, axis):
    me = lax.axis_index(axis)
    half = block.shape[1] // 2
    keep = lax.dynamic_slice_in_dim(block, me * half, half, 1)
    send = lax.dynamic_slice_in_dim(block, (1 - me) * half, half, 1)
    got = lax.ppermute(send, axis, [(0, 1), (1, 0)])
    return (keep.astype(jnp.float32) + got.astype(jnp.float32)).astype(block.dtype)


def exchange_scatter(rows, axis):
    size = lax.axis_size(axis)
    pieces = rows.reshape(size, rows.shape[0] // size, rows.shape[1])
    pieces = lax.all_to_all(pieces, axis, 0, 0, tiled=True)
    return pieces.astype(jnp.float32).sum(0).astype(rows.dtype)


def short_filter(extended, weights, count):
    lags = SHORT - 1
    total = jnp.zeros((extended.shape[0], count, extended.shape[2]), jnp.float32)
    for lag in range(SHORT):
        total = total + weights[:, lag, None, :] * extended[
            :, lags - lag : lags - lag + count, :
        ].astype(jnp.float32)
    return total


def banded_filters(filters, rows):
    local_groups = filters.shape[0]
    span = FLT - 1 + rows
    reversed_taps = jnp.flip(filters, axis=1)
    padded_taps = jnp.concatenate(
        [reversed_taps, jnp.zeros((local_groups, rows), filters.dtype)], axis=1
    )
    tiled = jnp.tile(padded_taps, (1, rows))
    return tiled[:, : rows * span].reshape(local_groups, rows, span)


def on_device(projected, taps, filters, skip, out_weight, positions):
    rows = projected.shape[1]
    width = projected.shape[2]
    lags = SHORT - 1
    reach = FLT - 1
    rim = shifted(projected[:, rows - lags :, :], "context", 1)
    feat = short_filter(jnp.concatenate([rim, projected], axis=1), taps, rows)
    query = feat[0]
    product = (feat[1] * feat[2]).astype(jnp.bfloat16)
    prior = shifted(product[rows - reach :], "context", 1)
    extended = jnp.concatenate([prior, product], axis=0)
    span = reach + rows
    toeplitz = banded_filters(filters, rows)
    local_groups = filters.shape[0]
    conv = jnp.einsum(
        "gim,mgc->igc",
        toeplitz,
        extended.reshape(span, local_groups, GROUP),
        preferred_element_type=jnp.float32,
    ).reshape(rows, width)
    conv = conv + skip[None, :] * product.astype(jnp.float32)
    gated = lax.optimization_barrier((query * conv).astype(jnp.bfloat16))
    offset = lax.axis_index("context") * rows
    local_sites = positions - offset
    one_hot = (local_sites[:, None] == jnp.arange(rows, dtype=jnp.int32)[None, :]).astype(
        jnp.bfloat16
    )
    picked_gated = jnp.dot(one_hot, gated, preferred_element_type=jnp.float32)
    site_gated = exchange_scatter(picked_gated.astype(jnp.bfloat16), "context")
    gated, site_gated = lax.optimization_barrier((gated, site_gated))
    full_weight = lax.all_gather(out_weight, "context", axis=1, tiled=True)
    terms = jnp.dot(gated, full_weight, preferred_element_type=jnp.float32)
    partial = lax.psum_scatter(terms.astype(jnp.bfloat16), "z", scatter_dimension=1, tiled=True)
    mixed = pair_scatter(partial, "x_lo")
    site_terms = jnp.dot(site_gated, full_weight, preferred_element_type=jnp.float32)
    site_terms = site_terms.astype(jnp.bfloat16)
    blocks = lax.axis_size(("z", "x_lo"))
    site_terms = site_terms.reshape(site_terms.shape[0], blocks, width).transpose(1, 0, 2)
    site_terms = lax.all_to_all(site_terms, ("z", "x_lo"), 0, 0, tiled=True)
    variant_states = site_terms.astype(jnp.float32).sum(0).astype(jnp.bfloat16)
    return (mixed, variant_states)


def split_mesh(mesh):
    devices = np.asarray(mesh.devices)
    context, tensor = devices.shape
    return Mesh(devices.reshape(context, tensor // 2, 2), ("context", "z", "x_lo"))


def solution(mesh):
    tensor = ("z", "x_lo")
    return jax.shard_map(
        on_device,
        mesh=split_mesh(mesh),
        in_specs=(
            P(None, "context", tensor),
            P(None, None, tensor),
            P(tensor, None),
            P(tensor),
            P(tensor, "context"),
            P(),
        ),
        out_specs=(P("context", tensor), P("context", tensor)),
        check_vma=False,
    )
```

```python
import jax
import jax.numpy as jnp
from jax import lax
import numpy as np
from jax.sharding import Mesh, PartitionSpec as P

FLT = 128
GROUP = 16
SHORT = 3


def shifted(array, axis, by):
    size = lax.axis_size(axis)
    pairs = [(i, i + by) for i in range(size) if 0 <= i + by < size]
    return lax.ppermute(array, axis, pairs)


def pair_scatter(block, axis):
    me = lax.axis_index(axis)
    half = block.shape[1] // 2
    keep = lax.dynamic_slice_in_dim(block, me * half, half, 1)
    send = lax.dynamic_slice_in_dim(block, (1 - me) * half, half, 1)
    got = lax.ppermute(send, axis, [(0, 1), (1, 0)])
    return (keep.astype(jnp.float32) + got.astype(jnp.float32)).astype(block.dtype)


def exchange_scatter(rows, axis):
    size = lax.axis_size(axis)
    pieces = rows.reshape(size, rows.shape[0] // size, rows.shape[1])
    pieces = lax.all_to_all(pieces, axis, 0, 0, tiled=True)
    return pieces.astype(jnp.float32).sum(0).astype(rows.dtype)


def short_filter(extended, weights, count):
    lags = SHORT - 1
    total = jnp.zeros((extended.shape[0], count, extended.shape[2]), jnp.float32)
    for lag in range(SHORT):
        total = total + weights[:, lag, None, :] * extended[
            :, lags - lag : lags - lag + count, :
        ].astype(jnp.float32)
    return total


def banded_filters(filters, rows):
    local_groups = filters.shape[0]
    span = FLT - 1 + rows
    reversed_taps = jnp.flip(filters, axis=1)
    padded_taps = jnp.concatenate(
        [reversed_taps, jnp.zeros((local_groups, rows), filters.dtype)], axis=1
    )
    tiled = jnp.tile(padded_taps, (1, rows))
    return tiled[:, : rows * span].reshape(local_groups, rows, span)


def on_device(projected, taps, filters, skip, out_weight, positions):
    rows = projected.shape[1]
    width = projected.shape[2]
    lags = SHORT - 1
    reach = FLT - 1
    rim = shifted(projected[:, rows - lags :, :], "context", 1)
    feat = short_filter(jnp.concatenate([rim, projected], axis=1), taps, rows)
    query = feat[0]
    product = (feat[1] * feat[2]).astype(jnp.bfloat16)
    prior = shifted(product[rows - reach :], "context", 1)
    extended = jnp.concatenate([prior, product], axis=0)
    span = reach + rows
    toeplitz = banded_filters(filters, rows)
    local_groups = filters.shape[0]
    conv = jnp.einsum(
        "gim,mgc->igc",
        toeplitz,
        extended.reshape(span, local_groups, GROUP),
        preferred_element_type=jnp.float32,
    ).reshape(rows, width)
    conv = conv + skip[None, :] * product.astype(jnp.float32)
    gated = lax.optimization_barrier((query * conv).astype(jnp.bfloat16))
    offset = lax.axis_index("context") * rows
    local_sites = positions - offset
    one_hot = (local_sites[:, None] == jnp.arange(rows, dtype=jnp.int32)[None, :]).astype(
        jnp.bfloat16
    )
    picked_gated = jnp.dot(one_hot, gated, preferred_element_type=jnp.float32)
    site_gated = exchange_scatter(picked_gated.astype(jnp.bfloat16), "context")
    gated, site_gated = lax.optimization_barrier((gated, site_gated))
    full_weight = lax.all_gather(out_weight, "context", axis=1, tiled=True)
    sites = site_gated.shape[0]
    padding = jnp.zeros((-(rows + sites) % 8, width), gated.dtype)
    both = jnp.concatenate([gated, site_gated, padding], axis=0)
    both = jnp.dot(both, full_weight, preferred_element_type=jnp.float32).astype(jnp.bfloat16)
    terms = both[:rows]
    site_terms = both[rows : rows + sites]
    partial = lax.psum_scatter(terms, "z", scatter_dimension=1, tiled=True)
    mixed = pair_scatter(partial, "x_lo")
    blocks = lax.axis_size(("z", "x_lo"))
    site_terms = site_terms.reshape(sites, blocks, width).transpose(1, 0, 2)
    site_terms = lax.all_to_all(site_terms, ("z", "x_lo"), 0, 0, tiled=True)
    variant_states = site_terms.astype(jnp.float32).sum(0).astype(jnp.bfloat16)
    return (mixed, variant_states)


def split_mesh(mesh):
    devices = np.asarray(mesh.devices)
    context, tensor = devices.shape
    return Mesh(devices.reshape(context, tensor // 2, 2), ("context", "z", "x_lo"))


def solution(mesh):
    tensor = ("z", "x_lo")
    return jax.shard_map(
        on_device,
        mesh=split_mesh(mesh),
        in_specs=(
            P(None, "context", tensor),
            P(None, None, tensor),
            P(tensor, None),
            P(tensor),
            P(tensor, "context"),
            P(),
        ),
        out_specs=(P("context", tensor), P("context", tensor)),
        check_vma=False,
    )
```

```python
import jax
import jax.numpy as jnp
from jax import lax
import numpy as np
from jax.sharding import Mesh, PartitionSpec as P

FLT = 128
GROUP = 16
SHORT = 3


def shifted(array, axis, by):
    size = lax.axis_size(axis)
    pairs = [(i, i + by) for i in range(size) if 0 <= i + by < size]
    return lax.ppermute(array, axis, pairs)


def pair_scatter(block, axis):
    me = lax.axis_index(axis)
    half = block.shape[1] // 2
    keep = lax.dynamic_slice_in_dim(block, me * half, half, 1)
    send = lax.dynamic_slice_in_dim(block, (1 - me) * half, half, 1)
    got = lax.ppermute(send, axis, [(0, 1), (1, 0)])
    return (keep.astype(jnp.float32) + got.astype(jnp.float32)).astype(block.dtype)


def exchange_scatter(rows, axis):
    size = lax.axis_size(axis)
    pieces = rows.reshape(size, rows.shape[0] // size, rows.shape[1])
    pieces = lax.all_to_all(pieces, axis, 0, 0, tiled=True)
    return pieces.astype(jnp.float32).sum(0).astype(rows.dtype)


def short_filter(extended, weights, count):
    lags = SHORT - 1
    total = jnp.zeros((extended.shape[0], count, extended.shape[2]), jnp.float32)
    for lag in range(SHORT):
        total = total + weights[:, lag, None, :] * extended[
            :, lags - lag : lags - lag + count, :
        ].astype(jnp.float32)
    return total


def banded_filters(filters, rows):
    local_groups = filters.shape[0]
    span = FLT - 1 + rows
    reversed_taps = jnp.flip(filters, axis=1)
    padded_taps = jnp.concatenate(
        [reversed_taps, jnp.zeros((local_groups, rows), filters.dtype)], axis=1
    )
    tiled = jnp.tile(padded_taps, (1, rows))
    return tiled[:, : rows * span].reshape(local_groups, rows, span)


def on_device(projected, taps, filters, skip, out_weight, positions):
    rows = projected.shape[1]
    width = projected.shape[2]
    lags = SHORT - 1
    reach = FLT - 1
    rim = shifted(projected[:, rows - lags :, :], "context", 1)
    feat = short_filter(jnp.concatenate([rim, projected], axis=1), taps, rows)
    query = feat[0]
    product = (feat[1] * feat[2]).astype(jnp.bfloat16)
    prior = shifted(product[rows - reach :], "context", 1)
    extended = jnp.concatenate([prior, product], axis=0)
    span = reach + rows
    toeplitz = banded_filters(filters, rows)
    local_groups = filters.shape[0]
    conv = jnp.einsum(
        "gim,mgc->igc",
        toeplitz,
        extended.reshape(span, local_groups, GROUP),
        preferred_element_type=jnp.float32,
    ).reshape(rows, width)
    conv = conv + skip[None, :] * product.astype(jnp.float32)
    gated = lax.optimization_barrier((query * conv).astype(jnp.bfloat16))
    offset = lax.axis_index("context") * rows
    local_sites = positions - offset
    one_hot = (local_sites[:, None] == jnp.arange(rows, dtype=jnp.int32)[None, :]).astype(
        jnp.bfloat16
    )
    picked_gated = jnp.dot(one_hot, gated, preferred_element_type=jnp.float32)
    site_gated = exchange_scatter(picked_gated.astype(jnp.bfloat16), "context")
    gated, site_gated = lax.optimization_barrier((gated, site_gated))
    full_weight = lax.all_gather(out_weight, "context", axis=1, tiled=True)
    sites = site_gated.shape[0]
    padding = jnp.zeros((-(rows + sites) % 8, width), gated.dtype)
    both = jnp.concatenate([gated, site_gated, padding], axis=0)
    both = jnp.dot(both, full_weight, preferred_element_type=jnp.float32).astype(jnp.bfloat16)
    partial = lax.psum_scatter(both, "z", scatter_dimension=1, tiled=True)
    reduced = pair_scatter(partial, "x_lo")
    mixed = reduced[:rows]
    variant_states = reduced[rows : rows + sites]
    return (mixed, variant_states)


def split_mesh(mesh):
    devices = np.asarray(mesh.devices)
    context, tensor = devices.shape
    return Mesh(devices.reshape(context, tensor // 2, 2), ("context", "z", "x_lo"))


def solution(mesh):
    tensor = ("z", "x_lo")
    return jax.shard_map(
        on_device,
        mesh=split_mesh(mesh),
        in_specs=(
            P(None, "context", tensor),
            P(None, None, tensor),
            P(tensor, None),
            P(tensor),
            P(tensor, "context"),
            P(),
        ),
        out_specs=(P("context", tensor), P("context", tensor)),
        check_vma=False,
    )
```

```python
import jax
import jax.numpy as jnp
from jax import lax
import numpy as np
from jax.sharding import Mesh, PartitionSpec as P

FLT = 128
GROUP = 16
SHORT = 3


def shifted(array, axis, by):
    size = lax.axis_size(axis)
    pairs = [(i, i + by) for i in range(size) if 0 <= i + by < size]
    return lax.ppermute(array, axis, pairs)


def pair_scatter(block, axis):
    me = lax.axis_index(axis)
    half = block.shape[1] // 2
    keep = lax.dynamic_slice_in_dim(block, me * half, half, 1)
    send = lax.dynamic_slice_in_dim(block, (1 - me) * half, half, 1)
    got = lax.ppermute(send, axis, [(0, 1), (1, 0)])
    return (keep.astype(jnp.float32) + got.astype(jnp.float32)).astype(block.dtype)


def exchange_scatter(rows, axis):
    size = lax.axis_size(axis)
    pieces = rows.reshape(size, rows.shape[0] // size, rows.shape[1])
    pieces = lax.all_to_all(pieces, axis, 0, 0, tiled=True)
    return pieces.astype(jnp.float32).sum(0).astype(rows.dtype)


def short_filter(extended, weights, count):
    lags = SHORT - 1
    total = jnp.zeros((extended.shape[0], count, extended.shape[2]), jnp.float32)
    for lag in range(SHORT):
        total = total + weights[:, lag, None, :] * extended[
            :, lags - lag : lags - lag + count, :
        ].astype(jnp.float32)
    return total


def banded_filters(filters, rows):
    local_groups = filters.shape[0]
    span = FLT - 1 + rows
    reversed_taps = jnp.flip(filters, axis=1)
    padded_taps = jnp.concatenate(
        [reversed_taps, jnp.zeros((local_groups, rows), filters.dtype)], axis=1
    )
    tiled = jnp.tile(padded_taps, (1, rows))
    return tiled[:, : rows * span].reshape(local_groups, rows, span)


def on_device(projected, taps, filters, skip, out_weight, positions):
    rows = projected.shape[1]
    width = projected.shape[2]
    lags = SHORT - 1
    reach = FLT - 1
    rim = shifted(projected[:, rows - lags :, :], "context", 1)
    feat = short_filter(jnp.concatenate([rim, projected], axis=1), taps, rows)
    query = feat[0]
    product = (feat[1] * feat[2]).astype(jnp.bfloat16)
    prior = shifted(product[rows - reach :], "context", 1)
    extended = jnp.concatenate([prior, product], axis=0)
    span = reach + rows
    toeplitz = banded_filters(filters, rows)
    local_groups = filters.shape[0]
    conv = jnp.einsum(
        "gim,mgc->igc",
        toeplitz,
        extended.reshape(span, local_groups, GROUP),
        preferred_element_type=jnp.float32,
    ).reshape(rows, width)
    conv = conv + skip[None, :] * product.astype(jnp.float32)
    gated = lax.optimization_barrier((query * conv).astype(jnp.bfloat16))
    offset = lax.axis_index("context") * rows
    local_sites = positions - offset
    one_hot = (local_sites[:, None] == jnp.arange(rows, dtype=jnp.int32)[None, :]).astype(
        jnp.bfloat16
    )
    picked_gated = jnp.dot(one_hot, gated, preferred_element_type=jnp.float32)
    site_gated = exchange_scatter(picked_gated.astype(jnp.bfloat16), "context")
    gated, site_gated = lax.optimization_barrier((gated, site_gated))
    full_weight = lax.all_gather(out_weight, "context", axis=1, tiled=True)
    sites = site_gated.shape[0]
    padding = jnp.zeros((-(rows + sites) % 8, width), gated.dtype)
    both = lax.optimization_barrier(jnp.concatenate([gated, site_gated, padding], axis=0))
    both = jnp.dot(both, full_weight, preferred_element_type=jnp.float32).astype(jnp.bfloat16)
    partial = lax.psum_scatter(both, "z", scatter_dimension=1, tiled=True)
    reduced = pair_scatter(partial, "x_lo")
    mixed = reduced[:rows]
    variant_states = reduced[rows : rows + sites]
    return (mixed, variant_states)


def split_mesh(mesh):
    devices = np.asarray(mesh.devices)
    context, tensor = devices.shape
    return Mesh(devices.reshape(context, tensor // 2, 2), ("context", "z", "x_lo"))


def solution(mesh):
    tensor = ("z", "x_lo")
    return jax.shard_map(
        on_device,
        mesh=split_mesh(mesh),
        in_specs=(
            P(None, "context", tensor),
            P(None, None, tensor),
            P(tensor, None),
            P(tensor),
            P(tensor, "context"),
            P(),
        ),
        out_specs=(P("context", tensor), P("context", tensor)),
        check_vma=False,
    )
```

```python
import jax
import jax.numpy as jnp
from jax import lax
import numpy as np
from jax.sharding import Mesh, PartitionSpec as P

FLT = 128
GROUP = 16
SHORT = 3


def shifted(array, axis, by):
    size = lax.axis_size(axis)
    pairs = [(i, i + by) for i in range(size) if 0 <= i + by < size]
    return lax.ppermute(array, axis, pairs)


def pair_scatter(block, axis):
    me = lax.axis_index(axis)
    half = block.shape[1] // 2
    keep = lax.dynamic_slice_in_dim(block, me * half, half, 1)
    send = lax.dynamic_slice_in_dim(block, (1 - me) * half, half, 1)
    got = lax.ppermute(send, axis, [(0, 1), (1, 0)])
    return (keep.astype(jnp.float32) + got.astype(jnp.float32)).astype(block.dtype)


def halving_scatter(rows, axis):
    size = lax.axis_size(axis)
    if size & (size - 1) or rows.shape[0] % size:
        return exchange_scatter(rows, axis)
    me = lax.axis_index(axis)
    step = size // 2
    while step >= 1:
        half = rows.shape[0] // 2
        bit = (me // step) % 2
        keep = lax.dynamic_slice_in_dim(rows, bit * half, half, 0)
        send = lax.dynamic_slice_in_dim(rows, (1 - bit) * half, half, 0)
        pairs = [(i, i ^ step) for i in range(size)]
        rows = keep + lax.ppermute(send, axis, pairs)
        step //= 2
    return rows


def exchange_scatter(rows, axis):
    size = lax.axis_size(axis)
    pieces = rows.reshape(size, rows.shape[0] // size, rows.shape[1])
    pieces = lax.all_to_all(pieces, axis, 0, 0, tiled=True)
    return pieces.astype(jnp.float32).sum(0).astype(rows.dtype)


def short_filter(extended, weights, count):
    lags = SHORT - 1
    total = jnp.zeros((extended.shape[0], count, extended.shape[2]), jnp.float32)
    for lag in range(SHORT):
        total = total + weights[:, lag, None, :] * extended[
            :, lags - lag : lags - lag + count, :
        ].astype(jnp.float32)
    return total


def banded_filters(filters, rows):
    local_groups = filters.shape[0]
    span = FLT - 1 + rows
    reversed_taps = jnp.flip(filters, axis=1)
    padded_taps = jnp.concatenate(
        [reversed_taps, jnp.zeros((local_groups, rows), filters.dtype)], axis=1
    )
    tiled = jnp.tile(padded_taps, (1, rows))
    return tiled[:, : rows * span].reshape(local_groups, rows, span)


def on_device(projected, taps, filters, skip, out_weight, positions):
    rows = projected.shape[1]
    width = projected.shape[2]
    lags = SHORT - 1
    reach = FLT - 1
    rim = shifted(projected[:, rows - lags :, :], "context", 1)
    feat = short_filter(jnp.concatenate([rim, projected], axis=1), taps, rows)
    query = feat[0]
    product = (feat[1] * feat[2]).astype(jnp.bfloat16)
    prior = shifted(product[rows - reach :], "context", 1)
    extended = jnp.concatenate([prior, product], axis=0)
    span = reach + rows
    toeplitz = banded_filters(filters, rows)
    local_groups = filters.shape[0]
    conv = jnp.einsum(
        "gim,mgc->igc",
        toeplitz,
        extended.reshape(span, local_groups, GROUP),
        preferred_element_type=jnp.float32,
    ).reshape(rows, width)
    conv = conv + skip[None, :] * product.astype(jnp.float32)
    gated = lax.optimization_barrier((query * conv).astype(jnp.bfloat16))
    offset = lax.axis_index("context") * rows
    local_sites = positions - offset
    one_hot = (local_sites[:, None] == jnp.arange(rows, dtype=jnp.int32)[None, :]).astype(
        jnp.bfloat16
    )
    picked_gated = jnp.dot(one_hot, gated, preferred_element_type=jnp.float32)
    site_gated = halving_scatter(picked_gated.astype(jnp.bfloat16), "context")
    gated, site_gated = lax.optimization_barrier((gated, site_gated))
    full_weight = lax.all_gather(out_weight, "context", axis=1, tiled=True)
    sites = site_gated.shape[0]
    padding = jnp.zeros((-(rows + sites) % 8, width), gated.dtype)
    both = jnp.concatenate([gated, site_gated, padding], axis=0)
    both = jnp.dot(both, full_weight, preferred_element_type=jnp.float32).astype(jnp.bfloat16)
    partial = lax.psum_scatter(both, "z", scatter_dimension=1, tiled=True)
    reduced = pair_scatter(partial, "x_lo")
    mixed = reduced[:rows]
    variant_states = reduced[rows : rows + sites]
    return (mixed, variant_states)


def split_mesh(mesh):
    devices = np.asarray(mesh.devices)
    context, tensor = devices.shape
    return Mesh(devices.reshape(context, tensor // 2, 2), ("context", "z", "x_lo"))


def solution(mesh):
    tensor = ("z", "x_lo")
    return jax.shard_map(
        on_device,
        mesh=split_mesh(mesh),
        in_specs=(
            P(None, "context", tensor),
            P(None, None, tensor),
            P(tensor, None),
            P(tensor),
            P(tensor, "context"),
            P(),
        ),
        out_specs=(P("context", tensor), P("context", tensor)),
        check_vma=False,
    )
```
